128 devices in a mesh: rows: 8 (over x, core), sub: 16 (over z, y).
Axes of the slice: x: 4, y: 4, z: 4, core: 2. Of those that a mesh axis runs over, the one named last changes fastest.
Arguments:
- vectors: float32 [262144, 1024], P(('rows', 'sub')), may hold values from -40 to 40
- list_ids: int32 [262144], P(('rows', 'sub')), may hold values from 0 to 1023
- coarse: float32 [1024, 1024], replicated, may hold values from -3 to 3
- rotation: float32 [1024, 1024], replicated, may hold values from -0.1875 to 0.1875
- codewords: float32 [16, 256, 64], P('sub'), may hold values from -6 to 6
Outputs:
- codebook: float32 [16, 256, 64], P('sub')
- distortion: float32 [16, 262144], P('sub', 'rows')
The draws below stay inside these ranges and needn't reach their ends.
All inputs are finite; a program needn't handle non-finite values.
Results may differ from the reference program's by a relative error of at most 0.0003.
Values sent between devices are 32-bit elements; how exact they have to be, the bound alone decides.
No kernel may reach another device: no remote copies, remote signals or barrier semaphores. Data moves between devices by JAX's collectives and lax.ppermute only.
A program may use at most 128 MiB of HBM per device.

```python
import math
import jax
import jax.numpy as jnp
from jax import lax

D = 1024
SUBS = 16
K = 256
NLIST = 1024
ITERS = 3
ROWS = 262144
DS = 64


def draw_vectors(key, part):
    first_key = jax.random.fold_in(key, 0)
    base = jax.random.normal(first_key, (ROWS, D), jnp.float32)
    return jnp.clip(base, -6.0, 6.0)


def plant(array, stream_key, low, top_value):
    spot = [jax.random.randint(jax.random.fold_in(stream_key, axis), (), 0, length) for axis, length in enumerate(array.shape)]
    widest = array.shape.index(max(array.shape))
    neighbour = spot[:widest] + [(spot[widest] + 1) % array.shape[widest]] + spot[widest + 1:]
    return array.at[tuple(spot)].set(low).at[tuple(neighbour)].set(top_value)


def block_scale(rng, extent, shards, smallest, high):
    gain = 1.0
    for axis_at, parts in shards:
        steps = jax.random.uniform(jax.random.fold_in(jax.random.fold_in(rng, 6), axis_at), (parts,), jnp.float32, smallest / len(shards), high / len(shards))
        gain = gain * jnp.repeat(jnp.exp(steps), extent[axis_at] // parts).reshape((-1,) + (1,) * (len(extent) - 1 - axis_at))
    return gain


def centred(rng, extent, spread, reach, cuts=(), kind=jnp.bfloat16):
    level = block_scale(rng, extent, cuts, -0.22, 0.18) if cuts else 1.0
    drawn = jax.random.normal(rng, extent, jnp.float32) * spread * level
    return jnp.minimum(jnp.maximum(drawn, -reach), reach).astype(kind)


def setup_inputs(seed: int = 0) -> dict:
    streams_of = jax.random.split(jax.random.key(seed), 6)
    vectors = draw_vectors(jax.random.fold_in(streams_of[5], 71), 0)
    list_ids = plant(jax.random.randint(streams_of[1], (ROWS,), 0, NLIST), jax.random.fold_in(streams_of[1], 1), 0, NLIST - 1).astype(jnp.int32)
    coarse = centred(streams_of[2], (NLIST, D), 0.5, 3.0, (), jnp.float32)
    rotation = centred(streams_of[3], (D, D), D ** -0.5, 0.1875, (), jnp.float32)
    codewords = centred(streams_of[4], (SUBS, K, DS), 1.0, 6.0, ((0, 16),), jnp.float32)
    return dict(vectors=vectors, list_ids=list_ids, coarse=coarse, rotation=rotation, codewords=codewords)


smoothing_factor = 16.0
pseudo_count = 1.0


def soft_stats(drawn_vectors_batch, codebook, requested_sums):
    row_count, sub_width = drawn_vectors_batch.shape
    block_rows = math.gcd(row_count, 2048)
    row_blocks = drawn_vectors_batch.reshape(row_count // block_rows, block_rows, sub_width)
    centroid_lengths = jnp.sum(codebook * codebook, axis=1)

    def accumulate(totals, row_block):
        products = jnp.dot(row_block, codebook.T, precision=lax.Precision.HIGHEST)
        quadratic_error = jnp.sum(row_block * row_block, axis=1, keepdims=True) - 2.0 * products + centroid_lengths[None, :]
        cluster_affinity_scores = -quadratic_error / smoothing_factor
        row_max = jnp.max(cluster_affinity_scores, axis=1, keepdims=True)
        unnormed = jnp.exp(cluster_affinity_scores - row_max)
        weights = unnormed / jnp.sum(unnormed, axis=1, keepdims=True)
        if requested_sums:
            membership_scaled = totals[0] + jnp.dot(weights.T, row_block, precision=lax.Precision.HIGHEST)
            masses = totals[1] + jnp.sum(weights, axis=0)
            return (membership_scaled, masses), None
        return totals, jnp.sum(weights * quadratic_error, axis=1) / sub_width

    start_sums = (jnp.zeros(codebook.shape, jnp.float32), jnp.zeros((codebook.shape[0],), jnp.float32))
    totals, per_row = lax.scan(accumulate, start_sums, row_blocks)
    if requested_sums:
        return totals
    return per_row.reshape(row_count)


def refit_codebook_entries(codebook, membership_scaled, masses):
    return (membership_scaled + pseudo_count * codebook) / (masses[..., None] + pseudo_count)


def reference(vectors, list_ids, coarse, rotation, codewords):
    residual = vectors - jnp.take(coarse, list_ids, axis=0)
    rotated = jnp.dot(residual, rotation, precision=lax.Precision.HIGHEST)
    drawn_vectors_batch = jnp.transpose(rotated.reshape(rotated.shape[0], SUBS, D // SUBS), (1, 0, 2))
    codebook = codewords
    for iteration in range(ITERS):
        membership_scaled, masses = lax.map(lambda operands: soft_stats(operands[0], operands[1], True), (drawn_vectors_batch, codebook))
        codebook = refit_codebook_entries(codebook, membership_scaled, masses)
    distortion = lax.map(lambda operands: soft_stats(operands[0], operands[1], False), (drawn_vectors_batch, codebook))
    return codebook, distortion
```

```python
import functools

import jax
import jax.numpy as jnp
from jax import lax
from jax.experimental import pallas as pl
from jax.experimental.pallas import tpu as pltpu
from jax.sharding import PartitionSpec as P

ITERS = 3
BLOCK = 2048

smoothing_factor = 16.0
pseudo_count = 1.0

HI = lax.Precision.HIGHEST


def _scores(c8_ref, bias_ref, xt):
    s = jnp.dot(c8_ref[...], xt, precision=HI, preferred_element_type=jnp.float32)
    return s - bias_ref[...]


def _stats_kernel(c8_ref, bias_ref, xt_ref, acc_ref):
    @pl.when(pl.program_id(0) == 0)
    def _():
        acc_ref[...] = jnp.zeros_like(acc_ref)

    xt = xt_ref[...]
    s = _scores(c8_ref, bias_ref, xt)
    m = jnp.max(s, axis=0, keepdims=True)
    e = jnp.exp(s - m)
    r = 1.0 / jnp.sum(e, axis=0, keepdims=True)
    y = jnp.concatenate([xt * r, jnp.broadcast_to(r, (8, xt.shape[1]))], axis=0)
    acc_ref[...] += lax.dot_general(
        e, y, (((1,), (1,)), ((), ())), precision=HI, preferred_element_type=jnp.float32
    )


def _dist_kernel(c8_ref, bias_ref, xt_ref, out_ref):
    xt = xt_ref[...]
    s = _scores(c8_ref, bias_ref, xt)
    m = jnp.max(s, axis=0, keepdims=True)
    e = jnp.exp(s - m)
    l = jnp.sum(e, axis=0, keepdims=True)
    t = jnp.sum(e * s, axis=0, keepdims=True)
    xx = jnp.sum(xt * xt, axis=0, keepdims=True)
    out_ref[...] = (xx - smoothing_factor * (t / l)) * (1.0 / xt.shape[0])


def _prep(codebook):
    c8 = codebook * 0.125
    bias = jnp.sum(codebook * codebook, axis=1, keepdims=True) * (1.0 / smoothing_factor)
    return c8, bias


def _specs(k, ds):
    return [
        pl.BlockSpec((k, ds), lambda i: (0, 0)),
        pl.BlockSpec((k, 1), lambda i: (0, 0)),
        pl.BlockSpec((ds, BLOCK), lambda i: (0, i)),
    ]


def soft_stats(xt, codebook):
    ds, n = xt.shape
    k = codebook.shape[0]
    c8, bias = _prep(codebook)
    return pl.pallas_call(
        _stats_kernel,
        grid=(n // BLOCK,),
        in_specs=_specs(k, ds),
        out_specs=pl.BlockSpec((k, ds + 8), lambda i: (0, 0)),
        out_shape=jax.ShapeDtypeStruct((k, ds + 8), jnp.float32),
        compiler_params=pltpu.CompilerParams(dimension_semantics=("arbitrary",)),
    )(c8, bias, xt)


def soft_distortion(xt, codebook):
    ds, n = xt.shape
    k = codebook.shape[0]
    c8, bias = _prep(codebook)
    return pl.pallas_call(
        _dist_kernel,
        grid=(n // BLOCK,),
        in_specs=_specs(k, ds),
        out_specs=pl.BlockSpec((1, BLOCK), lambda i: (0, i)),
        out_shape=jax.ShapeDtypeStruct((1, n), jnp.float32),
        compiler_params=pltpu.CompilerParams(dimension_semantics=("arbitrary",)),
    )(c8, bias, xt)


def tree_psum(x, axis, size):
    b = 1
    while b < size:
        x = x + lax.ppermute(x, axis, [(i, i ^ b) for i in range(size)])
        b *= 2
    return x


def per_device(vectors, list_ids, coarse, rotation, codewords, rows_size):
    residual = vectors - jnp.take(coarse, list_ids, axis=0)
    rotated_t = lax.dot_general(
        rotation, residual, (((0,), (1,)), ((), ())), precision=HI
    )
    xt = lax.all_to_all(rotated_t, "sub", split_axis=0, concat_axis=1, tiled=True)
    codebook = codewords[0]
    ds = codebook.shape[1]
    for iteration in range(ITERS):
        acc = soft_stats(xt, codebook)
        acc = tree_psum(acc, "rows", rows_size)
        membership_scaled = acc[:, :ds]
        masses = acc[:, ds]
        codebook = (membership_scaled + pseudo_count * codebook) / (
            masses[:, None] + pseudo_count
        )
    distortion = soft_distortion(xt, codebook)
    return (codebook[None], distortion)


def solution(mesh):
    in_specs = (P(("rows", "sub"), None), P(("rows", "sub")), P(), P(), P("sub", None, None))
    out_specs = (P("sub", None, None), P("sub", "rows"))
    return jax.shard_map(
        functools.partial(per_device, rows_size=mesh.shape["rows"]),
        mesh=mesh,
        in_specs=in_specs,
        out_specs=out_specs,
        check_vma=False,
    )
```

```python
import functools

import jax
import jax.numpy as jnp
from jax import lax
from jax.experimental import pallas as pl
from jax.experimental.pallas import tpu as pltpu
from jax.sharding import PartitionSpec as P

ITERS = 3
BLOCK = 2048

smoothing_factor = 16.0
pseudo_count = 1.0

HI = lax.Precision.HIGHEST


def _scores(c8_ref, bias_ref, xt):
    s = jnp.dot(c8_ref[...], xt, precision=HI, preferred_element_type=jnp.float32)
    return s - bias_ref[...]


def _split(a):
    hi = a.astype(jnp.bfloat16)
    return hi, (a - hi.astype(jnp.float32)).astype(jnp.bfloat16)


def _nt(a, b):
    return lax.dot_general(a, b, (((1,), (1,)), ((), ())), preferred_element_type=jnp.float32)


def _stats_kernel(c8_ref, bias_ref, xt_ref, acc_ref):
    @pl.when(pl.program_id(0) == 0)
    def _():
        acc_ref[...] = jnp.zeros_like(acc_ref)

    xt = xt_ref[...]
    s = _scores(c8_ref, bias_ref, xt)
    m = jnp.max(s, axis=0, keepdims=True)
    e = jnp.exp(s - m)
    r = 1.0 / jnp.sum(e, axis=0, keepdims=True)
    y = jnp.concatenate([xt * r, jnp.broadcast_to(r, (8, xt.shape[1]))], axis=0)
    eh, el = _split(e)
    yh, yl = _split(y)
    acc_ref[...] += _nt(eh, yh) + _nt(el, yh) + _nt(eh, yl)


def _dist_kernel(c8_ref, bias_ref, xt_ref, out_ref):
    xt = xt_ref[...]
    s = _scores(c8_ref, bias_ref, xt)
    m = jnp.max(s, axis=0, keepdims=True)
    e = jnp.exp(s - m)
    l = jnp.sum(e, axis=0, keepdims=True)
    t = jnp.sum(e * s, axis=0, keepdims=True)
    xx = jnp.sum(xt * xt, axis=0, keepdims=True)
    out_ref[...] = (xx - smoothing_factor * (t / l)) * (1.0 / xt.shape[0])


def _prep(codebook):
    c8 = codebook * 0.125
    bias = jnp.sum(codebook * codebook, axis=1, keepdims=True) * (1.0 / smoothing_factor)
    return c8, bias


def _specs(k, ds):
    return [
        pl.BlockSpec((k, ds), lambda i: (0, 0)),
        pl.BlockSpec((k, 1), lambda i: (0, 0)),
        pl.BlockSpec((ds, BLOCK), lambda i: (0, i)),
    ]


def soft_stats(xt, codebook):
    ds, n = xt.shape
    k = codebook.shape[0]
    c8, bias = _prep(codebook)
    return pl.pallas_call(
        _stats_kernel,
        grid=(n // BLOCK,),
        in_specs=_specs(k, ds),
        out_specs=pl.BlockSpec((k, ds + 8), lambda i: (0, 0)),
        out_shape=jax.ShapeDtypeStruct((k, ds + 8), jnp.float32),
        compiler_params=pltpu.CompilerParams(dimension_semantics=("arbitrary",)),
    )(c8, bias, xt)


def soft_distortion(xt, codebook):
    ds, n = xt.shape
    k = codebook.shape[0]
    c8, bias = _prep(codebook)
    return pl.pallas_call(
        _dist_kernel,
        grid=(n // BLOCK,),
        in_specs=_specs(k, ds),
        out_specs=pl.BlockSpec((1, BLOCK), lambda i: (0, i)),
        out_shape=jax.ShapeDtypeStruct((1, n), jnp.float32),
        compiler_params=pltpu.CompilerParams(dimension_semantics=("arbitrary",)),
    )(c8, bias, xt)


def gathered_psum(x, axis, size):
    parts = lax.all_to_all(
        jnp.broadcast_to(x[None], (size,) + x.shape), axis, 0, 0, tiled=True
    )
    total = parts[0]
    for j in range(1, size):
        total = total + parts[j]
    return total


def per_device(vectors, list_ids, coarse, rotation, codewords, rows_size):
    residual = vectors - jnp.take(coarse, list_ids, axis=0)
    rotated_t = lax.dot_general(
        rotation, residual, (((0,), (1,)), ((), ())), precision=HI
    )
    xt = lax.all_to_all(rotated_t, "sub", split_axis=0, concat_axis=1, tiled=True)
    codebook = codewords[0]
    ds = codebook.shape[1]
    for iteration in range(ITERS):
        acc = soft_stats(xt, codebook)
        acc = gathered_psum(acc, "rows", rows_size)
        membership_scaled = acc[:, :ds]
        masses = acc[:, ds]
        codebook = (membership_scaled + pseudo_count * codebook) / (
            masses[:, None] + pseudo_count
        )
    distortion = soft_distortion(xt, codebook)
    return (codebook[None], distortion)


def solution(mesh):
    in_specs = (P(("rows", "sub"), None), P(("rows", "sub")), P(), P(), P("sub", None, None))
    out_specs = (P("sub", None, None), P("sub", "rows"))
    return jax.shard_map(
        functools.partial(per_device, rows_size=mesh.shape["rows"]),
        mesh=mesh,
        in_specs=in_specs,
        out_specs=out_specs,
        check_vma=False,
    )
```

```python
import functools

import jax
import jax.numpy as jnp
from jax import lax
from jax.experimental import pallas as pl
from jax.experimental.pallas import tpu as pltpu
from jax.sharding import PartitionSpec as P

ITERS = 3
BLOCK = 4096
CHUNK_BLOCK = 1024
CHUNKS = 4

smoothing_factor = 16.0
pseudo_count = 1.0

HI = lax.Precision.HIGHEST


def _scores(c8_ref, bias_ref, xt):
    s = jnp.dot(c8_ref[...], xt, precision=HI, preferred_element_type=jnp.float32)
    return s - bias_ref[...]


def _split(a):
    hi = a.astype(jnp.bfloat16)
    return hi, (a - hi.astype(jnp.float32)).astype(jnp.bfloat16)


def _nt(a, b):
    return lax.dot_general(a, b, (((1,), (1,)), ((), ())), preferred_element_type=jnp.float32)


def _stats_body(c8_ref, bias_ref, xt, acc_ref):
    s = _scores(c8_ref, bias_ref, xt)
    m = jnp.max(s, axis=0, keepdims=True)
    e = jnp.exp(s - m)
    r = 1.0 / jnp.sum(e, axis=0, keepdims=True)
    y = jnp.concatenate([xt * r, jnp.broadcast_to(r, (8, xt.shape[1]))], axis=0)
    eh, el = _split(e)
    yh, yl = _split(y)
    acc_ref[...] += _nt(eh, yh) + _nt(el, yh) + _nt(eh, yl)


def _dist_body(c8_ref, bias_ref, xt, out_ref):
    s = _scores(c8_ref, bias_ref, xt)
    m = jnp.max(s, axis=0, keepdims=True)
    e = jnp.exp(s - m)
    l = jnp.sum(e, axis=0, keepdims=True)
    t = jnp.sum(e * s, axis=0, keepdims=True)
    xx = jnp.sum(xt * xt, axis=0, keepdims=True)
    out_ref[...] = (xx - smoothing_factor * (t / l)) * (1.0 / xt.shape[0])


def _prep(codebook):
    c8 = codebook * 0.125
    bias = jnp.sum(codebook * codebook, axis=1, keepdims=True) * (1.0 / smoothing_factor)
    return c8, bias


def _call(body, xt, codebook, out_spec, out_shape, zero_first, block):
    ds, n = xt.shape
    k = codebook.shape[0]
    c8, bias = _prep(codebook)

    def kernel(c8_ref, bias_ref, xt_ref, out_ref):
        if zero_first:
            @pl.when(pl.program_id(0) == 0)
            def _():
                out_ref[...] = jnp.zeros_like(out_ref)

        body(c8_ref, bias_ref, xt_ref[...], out_ref)

    return pl.pallas_call(
        kernel,
        grid=(n // block,),
        in_specs=[
            pl.BlockSpec((k, ds), lambda i: (0, 0)),
            pl.BlockSpec((k, 1), lambda i: (0, 0)),
            pl.BlockSpec((ds, block), lambda i: (0, i)),
        ],
        out_specs=out_spec,
        out_shape=out_shape,
        compiler_params=pltpu.CompilerParams(dimension_semantics=("arbitrary",)),
    )(c8, bias, xt)


def soft_stats(xt, codebook, block=BLOCK):
    ds = xt.shape[0]
    k = codebook.shape[0]
    return _call(
        _stats_body,
        xt,
        codebook,
        pl.BlockSpec((k, ds + 8), lambda i: (0, 0)),
        jax.ShapeDtypeStruct((k, ds + 8), jnp.float32),
        True,
        block,
    )


def soft_distortion(xt, codebook):
    n = xt.shape[1]
    return _call(
        _dist_body,
        xt,
        codebook,
        pl.BlockSpec((1, BLOCK), lambda i: (0, i)),
        jax.ShapeDtypeStruct((1, n), jnp.float32),
        False,
        BLOCK,
    )


def gathered_psum(x, axis, size):
    parts = lax.all_to_all(
        jnp.broadcast_to(x[None], (size,) + x.shape), axis, 0, 0, tiled=True
    )
    total = parts[0]
    for j in range(1, size):
        total = total + parts[j]
    return total


def per_device(vectors, list_ids, coarse, rotation, codewords, rows_size, chunks):
    local = vectors.shape[0]
    width = local // chunks
    codebook = codewords[0]
    ds = codebook.shape[1]
    xts = []
    acc = None
    for c in range(chunks):
        rows = slice(c * width, (c + 1) * width)
        residual = vectors[rows] - jnp.take(coarse, list_ids[rows], axis=0)
        rotated_t = lax.dot_general(
            rotation, residual, (((0,), (1,)), ((), ())), precision=HI
        )
        xt = lax.all_to_all(rotated_t, "sub", split_axis=0, concat_axis=1, tiled=True)
        xts.append(xt)
        part = soft_stats(xt, codebook, CHUNK_BLOCK)
        acc = part if acc is None else acc + part
    subs = xts[0].shape[1] // width
    xt = jnp.concatenate(xts, axis=1)
    def refit(codebook, acc):
        acc = gathered_psum(acc, "rows", rows_size)
        membership_scaled = acc[:, :ds]
        masses = acc[:, ds]
        return (membership_scaled + pseudo_count * codebook) / (masses[:, None] + pseudo_count)

    codebook = refit(codebook, acc)
    codebook = lax.fori_loop(
        1, ITERS, lambda _, codebook: refit(codebook, soft_stats(xt, codebook)), codebook
    )
    distortion = soft_distortion(xt, codebook)
    distortion = distortion.reshape(chunks, subs, width).transpose(1, 0, 2).reshape(1, -1)
    return (codebook[None], distortion)


def solution(mesh):
    in_specs = (P(("rows", "sub"), None), P(("rows", "sub")), P(), P(), P("sub", None, None))
    out_specs = (P("sub", None, None), P("sub", "rows"))
    return jax.shard_map(
        functools.partial(per_device, rows_size=mesh.shape["rows"], chunks=CHUNKS),
        mesh=mesh,
        in_specs=in_specs,
        out_specs=out_specs,
        check_vma=False,
    )
```

```python
import functools

import jax
import jax.numpy as jnp
from jax import lax
from jax.experimental import pallas as pl
from jax.experimental.pallas import tpu as pltpu
from jax.sharding import PartitionSpec as P

ITERS = 3
BLOCK = 4096
CHUNK_BLOCK = 1024
CHUNKS = 4

smoothing_factor = 16.0
pseudo_count = 1.0

HI = lax.Precision.HIGHEST


def _scores(c8_ref, bias_ref, xt):
    s = jnp.dot(c8_ref[...], xt, precision=HI, preferred_element_type=jnp.float32)
    return s - bias_ref[...]


def _split(a):
    hi = a.astype(jnp.bfloat16)
    return hi, (a - hi.astype(jnp.float32)).astype(jnp.bfloat16)


def _nt(a, b):
    return lax.dot_general(a, b, (((1,), (1,)), ((), ())), preferred_element_type=jnp.float32)


def _stats_body(c8_ref, bias_ref, xt, acc_ref):
    s = _scores(c8_ref, bias_ref, xt)
    m = jnp.max(s, axis=0, keepdims=True)
    e = jnp.exp(s - m)
    r = 1.0 / jnp.sum(e, axis=0, keepdims=True)
    y = jnp.concatenate([xt * r, jnp.broadcast_to(r, (8, xt.shape[1]))], axis=0)
    eh, el = _split(e)
    yh, yl = _split(y)
    acc_ref[...] += _nt(eh, yh) + _nt(el, yh) + _nt(eh, yl)


def _dist_body(c8_ref, bias_ref, xt, out_ref):
    s = _scores(c8_ref, bias_ref, xt)
    m = jnp.max(s, axis=0, keepdims=True)
    e = jnp.exp(s - m)
    l = jnp.sum(e, axis=0, keepdims=True)
    t = jnp.sum(e * s, axis=0, keepdims=True)
    xx = jnp.sum(xt * xt, axis=0, keepdims=True)
    out_ref[...] = (xx - smoothing_factor * (t / l)) * (1.0 / xt.shape[0])


def _prep(codebook):
    c8 = codebook * 0.125
    bias = jnp.sum(codebook * codebook, axis=1, keepdims=True) * (1.0 / smoothing_factor)
    return c8, bias


def _call(body, xt, codebook, out_spec, out_shape, zero_first, block):
    ds, n = xt.shape
    k = codebook.shape[0]
    c8, bias = _prep(codebook)

    def kernel(c8_ref, bias_ref, xt_ref, out_ref):
        if zero_first:
            @pl.when(pl.program_id(0) == 0)
            def _():
                out_ref[...] = jnp.zeros_like(out_ref)

        body(c8_ref, bias_ref, xt_ref[...], out_ref)

    return pl.pallas_call(
        kernel,
        grid=(n // block,),
        in_specs=[
            pl.BlockSpec((k, ds), lambda i: (0, 0)),
            pl.BlockSpec((k, 1), lambda i: (0, 0)),
            pl.BlockSpec((ds, block), lambda i: (0, i)),
        ],
        out_specs=out_spec,
        out_shape=out_shape,
        compiler_params=pltpu.CompilerParams(dimension_semantics=("arbitrary",)),
    )(c8, bias, xt)


def soft_stats(xt, codebook, block=BLOCK):
    ds = xt.shape[0]
    k = codebook.shape[0]
    return _call(
        _stats_body,
        xt,
        codebook,
        pl.BlockSpec((k, ds + 8), lambda i: (0, 0)),
        jax.ShapeDtypeStruct((k, ds + 8), jnp.float32),
        True,
        block,
    )


def soft_distortion(xt, codebook):
    n = xt.shape[1]
    return _call(
        _dist_body,
        xt,
        codebook,
        pl.BlockSpec((1, BLOCK), lambda i: (0, i)),
        jax.ShapeDtypeStruct((1, n), jnp.float32),
        False,
        BLOCK,
    )


def gathered_psum(x, axis, size):
    parts = lax.all_to_all(
        jnp.broadcast_to(x[None], (size,) + x.shape), axis, 0, 0, tiled=True
    )
    total = parts[0]
    for j in range(1, size):
        total = total + parts[j]
    return total


def per_device(vectors, list_ids, coarse, rotation, codewords, rows_size, chunks):
    local = vectors.shape[0]
    width = local // chunks
    codebook = codewords[0]
    ds = codebook.shape[1]
    xts = []
    parts = []
    for c in range(chunks):
        rows = slice(c * width, (c + 1) * width)
        residual = vectors[rows] - jnp.take(coarse, list_ids[rows], axis=0)
        if c >= 2:
            residual, parts[c - 2] = lax.optimization_barrier((residual, parts[c - 2]))
        rotated_t = lax.dot_general(
            rotation, residual, (((0,), (1,)), ((), ())), precision=HI
        )
        xt = lax.all_to_all(rotated_t, "sub", split_axis=0, concat_axis=1, tiled=True)
        xts.append(xt)
        parts.append(soft_stats(xt, codebook, CHUNK_BLOCK if c < chunks - 1 else BLOCK // 2))
    acc = parts[0]
    for part in parts[1:]:
        acc = acc + part
    subs = xts[0].shape[1] // width
    xt = jnp.concatenate(xts, axis=1)
    def refit(codebook, acc):
        acc = gathered_psum(acc, "rows", rows_size)
        membership_scaled = acc[:, :ds]
        masses = acc[:, ds]
        return (membership_scaled + pseudo_count * codebook) / (masses[:, None] + pseudo_count)

    codebook = refit(codebook, acc)
    codebook = lax.fori_loop(
        1, ITERS, lambda _, codebook: refit(codebook, soft_stats(xt, codebook)), codebook
    )
    distortion = soft_distortion(xt, codebook)
    distortion = distortion.reshape(chunks, subs, width).transpose(1, 0, 2).reshape(1, -1)
    return (codebook[None], distortion)


def solution(mesh):
    in_specs = (P(("rows", "sub"), None), P(("rows", "sub")), P(), P(), P("sub", None, None))
    out_specs = (P("sub", None, None), P("sub", "rows"))
    step = jax.shard_map(
        functools.partial(per_device, rows_size=mesh.shape["rows"], chunks=CHUNKS),
        mesh=mesh,
        in_specs=in_specs,
        out_specs=out_specs,
        check_vma=False,
    )
    return step
```

```python
import functools

import jax
import jax.numpy as jnp
from jax import lax
from jax.experimental import pallas as pl
from jax.experimental.pallas import tpu as pltpu
from jax.sharding import PartitionSpec as P

ITERS = 3
BLOCK = 4096
CHUNK_BLOCK = 2048
CHUNKS = 4

smoothing_factor = 16.0
pseudo_count = 1.0

HI = lax.Precision.HIGHEST
LOG2E = 1.4426950408889634


def _scores(c8_ref, bias_ref, xt):
    s = jnp.dot(c8_ref[...], xt, precision=HI, preferred_element_type=jnp.float32)
    return s - bias_ref[...]


def _split(a):
    hi = a.astype(jnp.bfloat16)
    return hi, (a - hi.astype(jnp.float32)).astype(jnp.bfloat16)


def _nt(a, b):
    return lax.dot_general(a, b, (((1,), (1,)), ((), ())), preferred_element_type=jnp.float32)


def _stats_body(c8_ref, bias_ref, xt, acc_ref):
    s = _scores(c8_ref, bias_ref, xt)
    m = jnp.max(s, axis=0, keepdims=True)
    e = jnp.exp2(s - m)
    r = 1.0 / jnp.sum(e, axis=0, keepdims=True)
    y = jnp.concatenate([xt * r, jnp.broadcast_to(r, (8, xt.shape[1]))], axis=0)
    eh, el = _split(e)
    yh, yl = _split(y)
    acc_ref[...] += _nt(eh, yh) + _nt(el, yh) + _nt(eh, yl)


def _dist_body(c8_ref, bias_ref, xt, out_ref):
    s = _scores(c8_ref, bias_ref, xt)
    m = jnp.max(s, axis=0, keepdims=True)
    e = jnp.exp2(s - m)
    l = jnp.sum(e, axis=0, keepdims=True)
    t = jnp.sum(e * s, axis=0, keepdims=True)
    xx = jnp.sum(xt * xt, axis=0, keepdims=True)
    out_ref[...] = (xx - (smoothing_factor / LOG2E) * (t / l)) * (1.0 / xt.shape[0])


def _prep(codebook):
    c8 = codebook * (2.0 * LOG2E / smoothing_factor)
    bias = jnp.sum(codebook * codebook, axis=1, keepdims=True) * (LOG2E / smoothing_factor)
    return c8, bias


def _call(body, xt, codebook, out_spec, out_shape, zero_first, block):
    ds, n = xt.shape
    k = codebook.shape[0]
    c8, bias = _prep(codebook)

    def kernel(c8_ref, bias_ref, xt_ref, out_ref):
        if zero_first:
            @pl.when(pl.program_id(0) == 0)
            def _():
                out_ref[...] = jnp.zeros_like(out_ref)

        body(c8_ref, bias_ref, xt_ref[...], out_ref)

    return pl.pallas_call(
        kernel,
        grid=(n // block,),
        in_specs=[
            pl.BlockSpec((k, ds), lambda i: (0, 0)),
            pl.BlockSpec((k, 1), lambda i: (0, 0)),
            pl.BlockSpec((ds, block), lambda i: (0, i)),
        ],
        out_specs=out_spec,
        out_shape=out_shape,
        compiler_params=pltpu.CompilerParams(dimension_semantics=("arbitrary",)),
    )(c8, bias, xt)


def soft_stats(xt, codebook, block=BLOCK):
    ds = xt.shape[0]
    k = codebook.shape[0]
    return _call(
        _stats_body,
        xt,
        codebook,
        pl.BlockSpec((k, ds + 8), lambda i: (0, 0)),
        jax.ShapeDtypeStruct((k, ds + 8), jnp.float32),
        True,
        block,
    )


def soft_distortion(xt, codebook):
    n = xt.shape[1]
    return _call(
        _dist_body,
        xt,
        codebook,
        pl.BlockSpec((1, BLOCK), lambda i: (0, i)),
        jax.ShapeDtypeStruct((1, n), jnp.float32),
        False,
        BLOCK,
    )


def gathered_psum(x, axis, size):
    parts = lax.all_to_all(
        jnp.broadcast_to(x[None], (size,) + x.shape), axis, 0, 0, tiled=True
    )
    total = parts[0]
    for j in range(1, size):
        total = total + parts[j]
    return total


def per_device(vectors, list_ids, coarse, rotation, codewords, rows_size, chunks):
    local = vectors.shape[0]
    width = local // chunks
    codebook = codewords[0]
    ds = codebook.shape[1]
    xts = []
    parts = []
    for c in range(chunks):
        rows = slice(c * width, (c + 1) * width)
        residual = vectors[rows] - jnp.take(coarse, list_ids[rows], axis=0)
        if c >= 2:
            residual, parts[c - 2] = lax.optimization_barrier((residual, parts[c - 2]))
        rotated_t = lax.dot_general(
            rotation, residual, (((0,), (1,)), ((), ())), precision=HI
        )
        xt = lax.all_to_all(rotated_t, "sub", split_axis=0, concat_axis=1, tiled=True)
        xts.append(xt)
        parts.append(soft_stats(xt, codebook, CHUNK_BLOCK))
    acc = parts[0]
    for part in parts[1:]:
        acc = acc + part
    subs = xts[0].shape[1] // width
    xt = jnp.concatenate(xts, axis=1)
    def refit(codebook, acc):
        acc = gathered_psum(acc, "rows", rows_size)
        membership_scaled = acc[:, :ds]
        masses = acc[:, ds]
        return (membership_scaled + pseudo_count * codebook) / (masses[:, None] + pseudo_count)

    codebook = refit(codebook, acc)
    codebook = lax.fori_loop(
        1, ITERS, lambda _, codebook: refit(codebook, soft_stats(xt, codebook)), codebook
    )
    distortion = soft_distortion(xt, codebook)
    distortion = distortion.reshape(chunks, subs, width).transpose(1, 0, 2).reshape(1, -1)
    return (codebook[None], distortion)


def solution(mesh):
    in_specs = (P(("rows", "sub"), None), P(("rows", "sub")), P(), P(), P("sub", None, None))
    out_specs = (P("sub", None, None), P("sub", "rows"))
    step = jax.shard_map(
        functools.partial(per_device, rows_size=mesh.shape["rows"], chunks=CHUNKS),
        mesh=mesh,
        in_specs=in_specs,
        out_specs=out_specs,
        check_vma=False,
    )
    return step
```

```python
import functools

import jax
import jax.numpy as jnp
from jax import lax
from jax.experimental import pallas as pl
from jax.experimental.pallas import tpu as pltpu
from jax.sharding import PartitionSpec as P

ITERS = 3
BLOCK = 4096
CHUNK_BLOCK = 2048
CHUNKS = 4

smoothing_factor = 16.0
pseudo_count = 1.0

HI = lax.Precision.HIGHEST
LOG2E = 1.4426950408889634


def _scores(c8_ref, bias_ref, xt):
    s = jnp.dot(c8_ref[...], xt, precision=HI, preferred_element_type=jnp.float32)
    return s - bias_ref[...]


def _split(a):
    hi = a.astype(jnp.bfloat16)
    return hi, (a - hi.astype(jnp.float32)).astype(jnp.bfloat16)


def _nt(a, b):
    return lax.dot_general(a, b, (((1,), (1,)), ((), ())), preferred_element_type=jnp.float32)


def _stats_body(c8_ref, bias_ref, xt, acc_ref):
    s = _scores(c8_ref, bias_ref, xt)
    m = jnp.max(s, axis=0, keepdims=True)
    e = jnp.exp2(s - m)
    r = 1.0 / jnp.sum(e, axis=0, keepdims=True)
    y = jnp.concatenate([xt * r, jnp.broadcast_to(r, (8, xt.shape[1]))], axis=0)
    eh, el = _split(e)
    yh, yl = _split(y)
    acc_ref[...] += _nt(eh, yh) + _nt(el, yh) + _nt(eh, yl)


def _dist_body(c8_ref, bias_ref, xt, out_ref):
    s = _scores(c8_ref, bias_ref, xt)
    m = jnp.max(s, axis=0, keepdims=True)
    e = jnp.exp2(s - m)
    l = jnp.sum(e, axis=0, keepdims=True)
    t = jnp.sum(e * s, axis=0, keepdims=True)
    xx = jnp.sum(xt * xt, axis=0, keepdims=True)
    out_ref[...] = (xx - (smoothing_factor / LOG2E) * (t / l)) * (1.0 / xt.shape[0])


def _prep(codebook):
    c8 = codebook * (2.0 * LOG2E / smoothing_factor)
    bias = jnp.sum(codebook * codebook, axis=1, keepdims=True) * (LOG2E / smoothing_factor)
    return c8, bias


def _call(body, xt, codebook, out_spec, out_shape, zero_first, block):
    ds, n = xt.shape
    k = codebook.shape[0]
    c8, bias = _prep(codebook)

    def kernel(c8_ref, bias_ref, xt_ref, out_ref):
        if zero_first:
            @pl.when(pl.program_id(0) == 0)
            def _():
                out_ref[...] = jnp.zeros_like(out_ref)

        body(c8_ref, bias_ref, xt_ref[...], out_ref)

    return pl.pallas_call(
        kernel,
        grid=(n // block,),
        in_specs=[
            pl.BlockSpec((k, ds), lambda i: (0, 0)),
            pl.BlockSpec((k, 1), lambda i: (0, 0)),
            pl.BlockSpec((ds, block), lambda i: (0, i)),
        ],
        out_specs=out_spec,
        out_shape=out_shape,
        compiler_params=pltpu.CompilerParams(dimension_semantics=("arbitrary",)),
    )(c8, bias, xt)


def soft_stats(xt, codebook, block=BLOCK):
    ds = xt.shape[0]
    k = codebook.shape[0]
    return _call(
        _stats_body,
        xt,
        codebook,
        pl.BlockSpec((k, ds + 8), lambda i: (0, 0)),
        jax.ShapeDtypeStruct((k, ds + 8), jnp.float32),
        True,
        block,
    )


def soft_distortion(xt, codebook):
    n = xt.shape[1]
    return _call(
        _dist_body,
        xt,
        codebook,
        pl.BlockSpec((1, BLOCK), lambda i: (0, i)),
        jax.ShapeDtypeStruct((1, n), jnp.float32),
        False,
        BLOCK,
    )


def gathered_psum(x, axis, size):
    got = [x] + [
        lax.ppermute(x, axis, [(i, (i + k) % size) for i in range(size)]) for k in range(1, size)
    ]
    by_shift = jnp.stack(got)
    me = lax.axis_index(axis)
    parts = jnp.take(by_shift, (me - jnp.arange(size)) % size, axis=0)
    total = parts[0]
    for j in range(1, size):
        total = total + parts[j]
    return total


def per_device(vectors, list_ids, coarse, rotation, codewords, rows_size, chunks):
    local = vectors.shape[0]
    width = local // chunks
    codebook = codewords[0]
    ds = codebook.shape[1]
    xts = []
    parts = []
    for c in range(chunks):
        rows = slice(c * width, (c + 1) * width)
        residual = vectors[rows] - jnp.take(coarse, list_ids[rows], axis=0)
        if c >= 2:
            residual, parts[c - 2] = lax.optimization_barrier((residual, parts[c - 2]))
        rotated_t = lax.dot_general(
            rotation, residual, (((0,), (1,)), ((), ())), precision=HI
        )
        xt = lax.all_to_all(rotated_t, "sub", split_axis=0, concat_axis=1, tiled=True)
        xts.append(xt)
        parts.append(soft_stats(xt, codebook, CHUNK_BLOCK))
    acc = parts[0]
    for part in parts[1:]:
        acc = acc + part
    subs = xts[0].shape[1] // width
    xt = jnp.concatenate(xts, axis=1)
    def refit(codebook, acc):
        acc = gathered_psum(acc, "rows", rows_size)
        membership_scaled = acc[:, :ds]
        masses = acc[:, ds]
        return (membership_scaled + pseudo_count * codebook) / (masses[:, None] + pseudo_count)

    codebook = refit(codebook, acc)
    codebook = lax.fori_loop(
        1, ITERS, lambda _, codebook: refit(codebook, soft_stats(xt, codebook)), codebook
    )
    distortion = soft_distortion(xt, codebook)
    distortion = distortion.reshape(chunks, subs, width).transpose(1, 0, 2).reshape(1, -1)
    return (codebook[None], distortion)


def solution(mesh):
    in_specs = (P(("rows", "sub"), None), P(("rows", "sub")), P(), P(), P("sub", None, None))
    out_specs = (P("sub", None, None), P("sub", "rows"))
    step = jax.shard_map(
        functools.partial(per_device, rows_size=mesh.shape["rows"], chunks=CHUNKS),
        mesh=mesh,
        in_specs=in_specs,
        out_specs=out_specs,
        check_vma=False,
    )
    return step
```

```python
import functools

import jax
import jax.numpy as jnp
from jax import lax
from jax.experimental import pallas as pl
from jax.experimental.pallas import tpu as pltpu
from jax.sharding import PartitionSpec as P

ITERS = 3
BLOCK = 4096
CHUNK_BLOCK = 2048
CHUNKS = 4

smoothing_factor = 16.0
pseudo_count = 1.0

HI = lax.Precision.HIGHEST
LOG2E = 1.4426950408889634


def _scores(c8_ref, bias_ref, xt):
    s = jnp.dot(c8_ref[...], xt, precision=HI, preferred_element_type=jnp.float32)
    return s - bias_ref[...]


def _split(a):
    hi = a.astype(jnp.bfloat16)
    return hi, (a - hi.astype(jnp.float32)).astype(jnp.bfloat16)


def _nt(a, b):
    return lax.dot_general(a, b, (((1,), (1,)), ((), ())), preferred_element_type=jnp.float32)


def _stats_body(c8_ref, bias_ref, xt, acc_ref):
    s = _scores(c8_ref, bias_ref, xt)
    m = jnp.max(s, axis=0, keepdims=True)
    e = jnp.exp2(s - m)
    r = 1.0 / jnp.sum(e, axis=0, keepdims=True)
    y = jnp.concatenate([xt * r, jnp.broadcast_to(r, (8, xt.shape[1]))], axis=0)
    eh, el = _split(e)
    yh, yl = _split(y)
    acc_ref[...] += _nt(eh, yh) + _nt(el, yh) + _nt(eh, yl)


def _dist_body(c8_ref, bias_ref, xt, out_ref):
    s = _scores(c8_ref, bias_ref, xt)
    m = jnp.max(s, axis=0, keepdims=True)
    e = jnp.exp2(s - m)
    l = jnp.sum(e, axis=0, keepdims=True)
    t = jnp.sum(e * s, axis=0, keepdims=True)
    xx = jnp.sum(xt * xt, axis=0, keepdims=True)
    out_ref[...] = (xx - (smoothing_factor / LOG2E) * (t / l)) * (1.0 / xt.shape[0])


def _prep(codebook):
    c8 = codebook * (2.0 * LOG2E / smoothing_factor)
    bias = jnp.sum(codebook * codebook, axis=1, keepdims=True) * (LOG2E / smoothing_factor)
    return c8, bias


def _call(body, xs, codebook, out_spec, out_shape, zero_first, block):
    slabs, ds, slab = xs.shape
    per = block // slab
    k = codebook.shape[0]
    c8, bias = _prep(codebook)

    def kernel(c8_ref, bias_ref, xs_ref, out_ref):
        if zero_first:
            @pl.when(pl.program_id(0) == 0)
            def _():
                out_ref[...] = jnp.zeros_like(out_ref)

        xt = jnp.concatenate([xs_ref[j] for j in range(per)], axis=1)
        body(c8_ref, bias_ref, xt, out_ref)

    return pl.pallas_call(
        kernel,
        grid=(slabs // per,),
        in_specs=[
            pl.BlockSpec((k, ds), lambda i: (0, 0)),
            pl.BlockSpec((k, 1), lambda i: (0, 0)),
            pl.BlockSpec((per, ds, slab), lambda i: (i, 0, 0)),
        ],
        out_specs=out_spec,
        out_shape=out_shape,
        compiler_params=pltpu.CompilerParams(dimension_semantics=("arbitrary",)),
    )(c8, bias, xs)


def soft_stats(xt, codebook, block=BLOCK):
    ds = xt.shape[1]
    k = codebook.shape[0]
    return _call(
        _stats_body,
        xt,
        codebook,
        pl.BlockSpec((k, ds + 8), lambda i: (0, 0)),
        jax.ShapeDtypeStruct((k, ds + 8), jnp.float32),
        True,
        block,
    )


def soft_distortion(xt, codebook):
    n = xt.shape[0] * xt.shape[2]
    return _call(
        _dist_body,
        xt,
        codebook,
        pl.BlockSpec((1, BLOCK), lambda i: (0, i)),
        jax.ShapeDtypeStruct((1, n), jnp.float32),
        False,
        BLOCK,
    )


def gathered_psum(x, axis, size):
    parts = lax.all_to_all(
        jnp.broadcast_to(x[None], (size,) + x.shape), axis, 0, 0, tiled=True
    )
    total = parts[0]
    for j in range(1, size):
        total = total + parts[j]
    return total


def per_device(vectors, list_ids, coarse, rotation, codewords, rows_size, chunks):
    local = vectors.shape[0]
    width = local // chunks
    codebook = codewords[0]
    ds = codebook.shape[1]
    xts = []
    parts = []
    for c in range(chunks):
        rows = slice(c * width, (c + 1) * width)
        residual = vectors[rows] - jnp.take(coarse, list_ids[rows], axis=0)
        if c >= 2:
            residual, parts[c - 2] = lax.optimization_barrier((residual, parts[c - 2]))
        rotated_t = lax.dot_general(
            rotation, residual, (((0,), (1,)), ((), ())), precision=HI
        )
        xt = lax.all_to_all(
            rotated_t.reshape(-1, ds, width), "sub", split_axis=0, concat_axis=0, tiled=True
        )
        xts.append(xt)
        parts.append(soft_stats(xt, codebook, CHUNK_BLOCK))
    acc = parts[0]
    for part in parts[1:]:
        acc = acc + part
    subs = xts[0].shape[0]
    xt = jnp.concatenate(xts, axis=0)
    def refit(codebook, acc):
        acc = gathered_psum(acc, "rows", rows_size)
        membership_scaled = acc[:, :ds]
        masses = acc[:, ds]
        return (membership_scaled + pseudo_count * codebook) / (masses[:, None] + pseudo_count)

    codebook = refit(codebook, acc)
    codebook = lax.fori_loop(
        1, ITERS, lambda _, codebook: refit(codebook, soft_stats(xt, codebook)), codebook
    )
    distortion = soft_distortion(xt, codebook)
    distortion = distortion.reshape(chunks, subs, width).transpose(1, 0, 2).reshape(1, -1)
    return (codebook[None], distortion)


def solution(mesh):
    in_specs = (P(("rows", "sub"), None), P(("rows", "sub")), P(), P(), P("sub", None, None))
    out_specs = (P("sub", None, None), P("sub", "rows"))
    step = jax.shard_map(
        functools.partial(per_device, rows_size=mesh.shape["rows"], chunks=CHUNKS),
        mesh=mesh,
        in_specs=in_specs,
        out_specs=out_specs,
        check_vma=False,
    )
    return step
```

```python
import functools

import jax
import jax.numpy as jnp
from jax import lax
from jax.experimental import pallas as pl
from jax.experimental.pallas import tpu as pltpu
from jax.sharding import PartitionSpec as P

ITERS = 3
BLOCK = 4096
CHUNK_BLOCK = 2048
CHUNKS = 2

smoothing_factor = 16.0
pseudo_count = 1.0

HI = lax.Precision.HIGHEST
LOG2E = 1.4426950408889634


def _scores(c8_ref, bias_ref, xt):
    s = jnp.dot(c8_ref[...], xt, precision=HI, preferred_element_type=jnp.float32)
    return s - bias_ref[...]


def _split(a):
    hi = a.astype(jnp.bfloat16)
    return hi, (a - hi.astype(jnp.float32)).astype(jnp.bfloat16)


def _nt(a, b):
    return lax.dot_general(a, b, (((1,), (1,)), ((), ())), preferred_element_type=jnp.float32)


def _stats_body(c8_ref, bias_ref, xt, acc_ref):
    s = _scores(c8_ref, bias_ref, xt)
    m = jnp.max(s, axis=0, keepdims=True)
    e = jnp.exp2(s - m)
    r = 1.0 / jnp.sum(e, axis=0, keepdims=True)
    y = jnp.concatenate([xt * r, jnp.broadcast_to(r, (8, xt.shape[1]))], axis=0)
    eh, el = _split(e)
    yh, yl = _split(y)
    acc_ref[...] += _nt(eh, yh) + _nt(el, yh) + _nt(eh, yl)


def _dist_body(c8_ref, bias_ref, xt, out_ref):
    s = _scores(c8_ref, bias_ref, xt)
    m = jnp.max(s, axis=0, keepdims=True)
    e = jnp.exp2(s - m)
    l = jnp.sum(e, axis=0, keepdims=True)
    t = jnp.sum(e * s, axis=0, keepdims=True)
    xx = jnp.sum(xt * xt, axis=0, keepdims=True)
    out_ref[...] = (xx - (smoothing_factor / LOG2E) * (t / l)) * (1.0 / xt.shape[0])


def _prep(codebook):
    c8 = codebook * (2.0 * LOG2E / smoothing_factor)
    bias = jnp.sum(codebook * codebook, axis=1, keepdims=True) * (LOG2E / smoothing_factor)
    return c8, bias


def _call(body, xs, codebook, out_spec, out_shape, zero_first, block):
    slabs, ds, slab = xs.shape
    per = block // slab
    k = codebook.shape[0]
    c8, bias = _prep(codebook)

    def kernel(c8_ref, bias_ref, xs_ref, out_ref):
        if zero_first:
            @pl.when(pl.program_id(0) == 0)
            def _():
                out_ref[...] = jnp.zeros_like(out_ref)

        xt = jnp.concatenate([xs_ref[j] for j in range(per)], axis=1)
        body(c8_ref, bias_ref, xt, out_ref)

    return pl.pallas_call(
        kernel,
        grid=(slabs // per,),
        in_specs=[
            pl.BlockSpec((k, ds), lambda i: (0, 0)),
            pl.BlockSpec((k, 1), lambda i: (0, 0)),
            pl.BlockSpec((per, ds, slab), lambda i: (i, 0, 0)),
        ],
        out_specs=out_spec,
        out_shape=out_shape,
        compiler_params=pltpu.CompilerParams(dimension_semantics=("arbitrary",)),
    )(c8, bias, xs)


def soft_stats(xt, codebook, block=BLOCK):
    ds = xt.shape[1]
    k = codebook.shape[0]
    return _call(
        _stats_body,
        xt,
        codebook,
        pl.BlockSpec((k, ds + 8), lambda i: (0, 0)),
        jax.ShapeDtypeStruct((k, ds + 8), jnp.float32),
        True,
        block,
    )


def soft_distortion(xt, codebook):
    n = xt.shape[0] * xt.shape[2]
    return _call(
        _dist_body,
        xt,
        codebook,
        pl.BlockSpec((1, BLOCK), lambda i: (0, i)),
        jax.ShapeDtypeStruct((1, n), jnp.float32),
        False,
        BLOCK,
    )


def gathered_psum(x, axis, size):
    parts = lax.all_to_all(
        jnp.broadcast_to(x[None], (size,) + x.shape), axis, 0, 0, tiled=True
    )
    total = parts[0]
    for j in range(1, size):
        total = total + parts[j]
    return total


def per_device(vectors, list_ids, coarse, rotation, codewords, rows_size, chunks):
    local = vectors.shape[0]
    width = local // chunks
    codebook = codewords[0]
    ds = codebook.shape[1]
    xts = []
    parts = []
    for c in range(chunks):
        rows = slice(c * width, (c + 1) * width)
        residual = vectors[rows] - jnp.take(coarse, list_ids[rows], axis=0)
        if c >= 2:
            residual, parts[c - 2] = lax.optimization_barrier((residual, parts[c - 2]))
        rotated_t = lax.dot_general(
            rotation, residual, (((0,), (1,)), ((), ())), precision=HI
        )
        xt = lax.all_to_all(
            rotated_t.reshape(-1, ds, width), "sub", split_axis=0, concat_axis=0, tiled=True
        )
        xts.append(xt)
        parts.append(soft_stats(xt, codebook, CHUNK_BLOCK))
    acc = parts[0]
    for part in parts[1:]:
        acc = acc + part
    subs = xts[0].shape[0]
    xt = jnp.concatenate(xts, axis=0)
    def refit(codebook, acc):
        acc = gathered_psum(acc, "rows", rows_size)
        membership_scaled = acc[:, :ds]
        masses = acc[:, ds]
        return (membership_scaled + pseudo_count * codebook) / (masses[:, None] + pseudo_count)

    codebook = refit(codebook, acc)
    codebook = lax.fori_loop(
        1, ITERS, lambda _, codebook: refit(codebook, soft_stats(xt, codebook)), codebook
    )
    distortion = soft_distortion(xt, codebook)
    distortion = distortion.reshape(chunks, subs, width).transpose(1, 0, 2).reshape(1, -1)
    return (codebook[None], distortion)


def solution(mesh):
    in_specs = (P(("rows", "sub"), None), P(("rows", "sub")), P(), P(), P("sub", None, None))
    out_specs = (P("sub", None, None), P("sub", "rows"))
    step = jax.shard_map(
        functools.partial(per_device, rows_size=mesh.shape["rows"], chunks=CHUNKS),
        mesh=mesh,
        in_specs=in_specs,
        out_specs=out_specs,
        check_vma=False,
    )
    return step
```

```python
import functools

import jax
import jax.numpy as jnp
from jax import lax
from jax.experimental import pallas as pl
from jax.experimental.pallas import tpu as pltpu
from jax.sharding import PartitionSpec as P

ITERS = 3
BLOCK = 4096
CHUNK_BLOCK = 1024
CHUNKS = 2

smoothing_factor = 16.0
pseudo_count = 1.0

HI = lax.Precision.HIGHEST
LOG2E = 1.4426950408889634


def _scores(c8_ref, bias_ref, xt):
    s = jnp.dot(c8_ref[...], xt, precision=HI, preferred_element_type=jnp.float32)
    return s - bias_ref[...]


def _split(a):
    hi = a.astype(jnp.bfloat16)
    return hi, (a - hi.astype(jnp.float32)).astype(jnp.bfloat16)


def _nt(a, b):
    return lax.dot_general(a, b, (((1,), (1,)), ((), ())), preferred_element_type=jnp.float32)


def _stats_body(c8_ref, bias_ref, xt, acc_ref):
    s = _scores(c8_ref, bias_ref, xt)
    m = jnp.max(s, axis=0, keepdims=True)
    e = jnp.exp2(s - m)
    r = 1.0 / jnp.sum(e, axis=0, keepdims=True)
    y = jnp.concatenate([xt * r, jnp.broadcast_to(r, (8, xt.shape[1]))], axis=0)
    eh, el = _split(e)
    yh, yl = _split(y)
    acc_ref[...] += _nt(eh, yh) + _nt(el, yh) + _nt(eh, yl)


def _dist_body(c8_ref, bias_ref, xt, out_ref):
    s = _scores(c8_ref, bias_ref, xt)
    m = jnp.max(s, axis=0, keepdims=True)
    e = jnp.exp2(s - m)
    l = jnp.sum(e, axis=0, keepdims=True)
    t = jnp.sum(e * s, axis=0, keepdims=True)
    xx = jnp.sum(xt * xt, axis=0, keepdims=True)
    out_ref[...] = (xx - (smoothing_factor / LOG2E) * (t / l)) * (1.0 / xt.shape[0])


def _prep(codebook):
    c8 = codebook * (2.0 * LOG2E / smoothing_factor)
    bias = jnp.sum(codebook * codebook, axis=1, keepdims=True) * (LOG2E / smoothing_factor)
    return c8, bias


def _call(body, xs, codebook, out_spec, out_shape, zero_first, block):
    slabs, ds, slab = xs.shape
    per = block // slab
    k = codebook.shape[0]
    c8, bias = _prep(codebook)

    def kernel(c8_ref, bias_ref, xs_ref, out_ref):
        if zero_first:
            @pl.when(pl.program_id(0) == 0)
            def _():
                out_ref[...] = jnp.zeros_like(out_ref)

        xt = jnp.concatenate([xs_ref[j] for j in range(per)], axis=1)
        body(c8_ref, bias_ref, xt, out_ref)

    return pl.pallas_call(
        kernel,
        grid=(slabs // per,),
        in_specs=[
            pl.BlockSpec((k, ds), lambda i: (0, 0)),
            pl.BlockSpec((k, 1), lambda i: (0, 0)),
            pl.BlockSpec((per, ds, slab), lambda i: (i, 0, 0)),
        ],
        out_specs=out_spec,
        out_shape=out_shape,
        compiler_params=pltpu.CompilerParams(dimension_semantics=("arbitrary",)),
    )(c8, bias, xs)


def soft_stats(xt, codebook, block=BLOCK):
    ds = xt.shape[1]
    k = codebook.shape[0]
    return _call(
        _stats_body,
        xt,
        codebook,
        pl.BlockSpec((k, ds + 8), lambda i: (0, 0)),
        jax.ShapeDtypeStruct((k, ds + 8), jnp.float32),
        True,
        block,
    )


def soft_distortion(xt, codebook):
    n = xt.shape[0] * xt.shape[2]
    return _call(
        _dist_body,
        xt,
        codebook,
        pl.BlockSpec((1, BLOCK), lambda i: (0, i)),
        jax.ShapeDtypeStruct((1, n), jnp.float32),
        False,
        BLOCK,
    )


def gathered_psum(x, axis, size):
    parts = lax.all_to_all(
        jnp.broadcast_to(x[None], (size,) + x.shape), axis, 0, 0, tiled=True
    )
    total = parts[0]
    for j in range(1, size):
        total = total + parts[j]
    return total


def per_device(vectors, list_ids, coarse, rotation, codewords, rows_size, chunks):
    local = vectors.shape[0]
    width = local // chunks
    codebook = codewords[0]
    ds = codebook.shape[1]
    xts = []
    parts = []
    for c in range(chunks):
        rows = slice(c * width, (c + 1) * width)
        residual = vectors[rows] - jnp.take(coarse, list_ids[rows], axis=0)
        if c >= 2:
            residual, parts[c - 2] = lax.optimization_barrier((residual, parts[c - 2]))
        rotated_t = lax.dot_general(
            rotation, residual, (((0,), (1,)), ((), ())), precision=HI
        )
        xt = lax.all_to_all(
            rotated_t.reshape(-1, ds, width), "sub", split_axis=0, concat_axis=0, tiled=True
        )
        xts.append(xt)
        parts.append(soft_stats(xt, codebook, BLOCK if c == chunks - 1 else CHUNK_BLOCK))
    acc = parts[0]
    for part in parts[1:]:
        acc = acc + part
    subs = xts[0].shape[0]
    xt = jnp.concatenate(xts, axis=0)
    def refit(codebook, acc):
        acc = gathered_psum(acc, "rows", rows_size)
        membership_scaled = acc[:, :ds]
        masses = acc[:, ds]
        return (membership_scaled + pseudo_count * codebook) / (masses[:, None] + pseudo_count)

    codebook = refit(codebook, acc)
    codebook = lax.fori_loop(
        1, ITERS, lambda _, codebook: refit(codebook, soft_stats(xt, codebook)), codebook
    )
    distortion = soft_distortion(xt, codebook)
    distortion = distortion.reshape(chunks, subs, width).transpose(1, 0, 2).reshape(1, -1)
    return (codebook[None], distortion)


def solution(mesh):
    in_specs = (P(("rows", "sub"), None), P(("rows", "sub")), P(), P(), P("sub", None, None))
    out_specs = (P("sub", None, None), P("sub", "rows"))
    step = jax.shard_map(
        functools.partial(per_device, rows_size=mesh.shape["rows"], chunks=CHUNKS),
        mesh=mesh,
        in_specs=in_specs,
        out_specs=out_specs,
        check_vma=False,
    )
    return step
```
